512 devices in a mesh: blk: 32 (over z, y_lo), rep: 16 (over x, y_hi, core).
Axes of the slice: x: 4, y: 4 (y_hi: 2, y_lo: 2; y = y_hi * 2 + y_lo), z: 16, core: 2. Of those that a mesh axis runs over, the one named last changes fastest.
Arguments:
- feats: bfloat16 [32768, 256], P(('blk', 'rep')), may hold values from -6 to 6
- weight: bfloat16 [256, 256], replicated, may hold values from -0.375 to 0.375
- bias: float32 [256], replicated, may hold values from -4 to 4
- grad_out: bfloat16 [32768, 256], P(('blk', 'rep')), may hold values from -6 to 6
- tile_values: bfloat16 [32, 16, 2, 64, 128, 128], P('blk', 'rep'), may hold values from -0.03125 to 0.03125
- tile_rows: int32 [32, 16, 2, 64], P('blk', 'rep'), may hold values from 0 to 7, as said below
- tile_cols: int32 [32, 16, 2, 64], P('blk', 'rep'), may hold values from 0 to 7, as said below
- tile_count: int32 [32, 16, 2], P('blk', 'rep'), may hold values from 32 to 64, as said below
Outputs:
- out: bfloat16 [32768, 256], P(('blk', 'rep'))
- grad_feats: bfloat16 [32768, 256], P(('blk', 'rep'))
- grad_weight: float32 [256, 256], P('rep')
- grad_bias: float32 [256], replicated
The draws below stay inside these ranges and needn't reach their ends.
Inputs may be any that keep to these rules, and one draw needn't show every extreme that they name: `tile_count`: some pair slot of some device holds exactly 64 live entries; slots past the count hold values that must be ignored. Within one pair slot the 64 entries name distinct (tile_rows, tile_cols) cells. `tile_cols`: see tile_rows: cells of one slot are distinct.
All inputs are finite; a program needn't handle non-finite values.
Results may differ from the reference program's by a relative error of at most 0.018.
Values may be sent and summed in bfloat16 or wider, within the bound.
No kernel may reach another device: no remote copies, remote signals or barrier semaphores. Data moves between devices by JAX's collectives and lax.ppermute only.
A program may use at most 64 MiB of HBM per device.

```python
import jax
import jax.numpy as jnp
from jax import lax

F = 256
TILE = 128
MAXT = 64
TILES_P = 8
ROWS_DEV = 64
PAIRS_DEV = 2
NODES = 32768
N_BLK = 32
N_REP = 16


def draw_tile_count(key, part):
    first_key, second_key = jax.random.split(jax.random.fold_in(key, 17))
    entries = N_BLK * N_REP * PAIRS_DEV
    counts = jax.random.randint(first_key, (entries,), MAXT // 2, MAXT + 1, dtype=jnp.int32)
    chosen = jax.random.randint(second_key, (), 0, entries, dtype=jnp.int32)
    counts = counts.at[chosen].set(MAXT)
    return counts.reshape(N_BLK, N_REP, PAIRS_DEV)


def tile_cells(key):
    first_key, second_key = jax.random.split(jax.random.fold_in(key, 23))
    slot_total = N_BLK * N_REP * PAIRS_DEV
    cell_total = TILES_P * TILES_P
    cell_index = jnp.arange(cell_total, dtype=jnp.int32)
    scores = jax.random.randint(first_key, (slot_total, cell_total), 0, 2 ** 20, dtype=jnp.int32)
    scores = scores * cell_total + cell_index[None, :]
    chosen = jax.random.randint(second_key, (), 0, slot_total, dtype=jnp.int32)
    slot_index = jnp.arange(slot_total, dtype=jnp.int32)
    planted = (slot_index[:, None] == chosen) & ((cell_index == 0) | (cell_index == cell_total - 1))[None, :]
    scores = jnp.where(planted, (cell_index - cell_total)[None, :], scores)
    order = jnp.argsort(scores, axis=1)[:, :MAXT].astype(jnp.int32)
    return order.reshape(N_BLK, N_REP, PAIRS_DEV, MAXT)


def draw_tile_rows(key, part):
    return tile_cells(key) // TILES_P


def draw_tile_cols(key, part):
    return tile_cells(key) % TILES_P


def levels(stream_key, shape, cuts, low, high):
    loudness = 1.0
    for dim, blocks in cuts:
        draws = jax.random.uniform(jax.random.fold_in(jax.random.fold_in(stream_key, 6), dim), (blocks,), jnp.float32, low / len(cuts), high / len(cuts))
        loudness = loudness * jnp.repeat(jnp.exp(draws), shape[dim] // blocks).reshape((-1,) + (1,) * (len(shape) - 1 - dim))
    return loudness


def scatter_about(stream_key, extent, width, reach, pieces=(), held_as=jnp.bfloat16):
    values = jax.random.normal(stream_key, extent, jnp.float32) * width
    if len(pieces) > 0:
        values = levels(stream_key, extent, pieces, -0.22, 0.18) * values
    return jnp.clip(values, min=-reach, max=reach).astype(held_as)


def setup_inputs(seed: int = 0) -> dict:
    seeds = jax.random.split(jax.random.key(seed), 9)
    feats = scatter_about(seeds[0], (NODES, F), 1.0, 6.0, ((0, 512),))
    weight = scatter_about(seeds[1], (F, F), F ** -0.5, 0.375)
    bias = scatter_about(seeds[2], (F,), 1.0, 4.0, (), jnp.float32)
    grad_out = scatter_about(seeds[3], (NODES, F), 1.0, 6.0, ((0, 512),))
    tile_values = scatter_about(seeds[4], (N_BLK, N_REP, PAIRS_DEV, MAXT, TILE, TILE), (TILE * MAXT * N_BLK // TILES_P) ** -0.5, 0.03125, ((0, 32), (1, 16)))
    tile_rows = draw_tile_rows(jax.random.fold_in(seeds[8], 71), 0)
    tile_cols = draw_tile_cols(jax.random.fold_in(seeds[8], 71), 0)
    tile_count = draw_tile_count(jax.random.fold_in(seeds[8], 71), 0)
    return {"feats": feats, "weight": weight, "bias": bias, "grad_out": grad_out, "tile_values": tile_values, "tile_rows": tile_rows, "tile_cols": tile_cols, "tile_count": tile_count}


def forward_tiles(total, source, tile_vals, tile_row, tile_col, live, tile_size):
    def one_tile(position, total):
        row_start = tile_row[position] * tile_size
        col_start = tile_col[position] * tile_size
        source_rows = lax.dynamic_slice_in_dim(source, col_start, tile_size, 0)
        current = lax.dynamic_slice_in_dim(total, row_start, tile_size, 0)
        current = current + jnp.dot(tile_vals[position], source_rows, preferred_element_type=jnp.float32)
        return lax.dynamic_update_slice_in_dim(total, current, row_start, 0)
    return lax.fori_loop(0, live, one_tile, total)


def reference(feats, weight, bias, grad_out, tile_values, tile_rows, tile_cols, tile_count):
    part_rows = ROWS_DEV * N_REP
    pair_total = N_REP * PAIRS_DEV
    hw_full = jnp.dot(feats, weight, preferred_element_type=jnp.float32).astype(jnp.bfloat16)
    hw_blocks = hw_full.reshape(N_BLK, part_rows, F)

    def forward_part(part_index):
        def pair_step(total, flat):
            replica = flat // PAIRS_DEV
            slot = flat % PAIRS_DEV
            source_part = (part_index - replica - slot * N_REP) % N_BLK
            source = lax.dynamic_index_in_dim(hw_blocks, source_part, 0, keepdims=False)
            total = forward_tiles(total, source, tile_values[part_index, replica, slot],
                                  tile_rows[part_index, replica, slot], tile_cols[part_index, replica, slot],
                                  tile_count[part_index, replica, slot], TILE)
            return total, None
        total, _ = lax.scan(pair_step, jnp.zeros((part_rows, F), jnp.float32), jnp.arange(pair_total, dtype=jnp.int32))
        return total

    aggregate = lax.map(forward_part, jnp.arange(N_BLK, dtype=jnp.int32)).reshape(NODES, F)
    pre_act = aggregate + bias
    logistic = jax.nn.sigmoid(pre_act)
    out = (pre_act * logistic).astype(jnp.bfloat16)
    grad_pre = (grad_out.astype(jnp.float32) * logistic * (1.0 + pre_act * (1.0 - logistic))).astype(jnp.bfloat16)

    def backward_step(total, flat):
        part_index = flat // pair_total
        pair_flat = flat % pair_total
        replica = pair_flat // PAIRS_DEV
        slot = pair_flat % PAIRS_DEV
        source_part = (part_index - replica - slot * N_REP) % N_BLK
        tile_vals = tile_values[part_index, replica, slot]
        tile_row = tile_rows[part_index, replica, slot]
        tile_col = tile_cols[part_index, replica, slot]

        def one_tile(position, total):
            row_start = part_index * part_rows + tile_row[position] * TILE
            col_start = source_part * part_rows + tile_col[position] * TILE
            grad_rows = lax.dynamic_slice_in_dim(grad_pre, row_start, TILE, 0)
            term = lax.dot_general(tile_vals[position], grad_rows, (((0,), (0,)), ((), ())),
                                   preferred_element_type=jnp.float32)
            current = lax.dynamic_slice_in_dim(total, col_start, TILE, 0)
            return lax.dynamic_update_slice_in_dim(total, current + term, col_start, 0)
        total = lax.fori_loop(0, tile_count[part_index, replica, slot], one_tile, total)
        return total, None

    grad_total, _ = lax.scan(backward_step, jnp.zeros((NODES, F), jnp.float32),
                             jnp.arange(N_BLK * pair_total, dtype=jnp.int32))
    grad_hw = grad_total.astype(jnp.bfloat16)
    grad_feats = lax.dot_general(grad_hw, weight, (((1,), (1,)), ((), ())),
                                 preferred_element_type=jnp.float32).astype(jnp.bfloat16)
    grad_weight = lax.dot_general(feats, grad_hw, (((0,), (0,)), ((), ())), preferred_element_type=jnp.float32)
    grad_bias = jnp.sum(grad_pre.astype(jnp.float32), axis=0)
    return (out, grad_feats, grad_weight, grad_bias)
```

```python
import jax
import jax.numpy as jnp
from jax import lax
from jax.sharding import PartitionSpec as P


def passed_along(x, axis, by):
    devices = lax.axis_size(axis)
    return lax.ppermute(x, axis, [(i, (i + by) % devices) for i in range(devices)])


def dense_adjacency(tile_vals, tile_row, tile_col, live, tiles_per_part):
    entries, tile_size, _ = tile_vals.shape
    cells = tiles_per_part * tiles_per_part
    cell_of_entry = tile_row * tiles_per_part + tile_col
    alive = jnp.arange(entries) < live
    select = (cell_of_entry[None, :] == jnp.arange(cells)[:, None]) & alive[None, :]
    placed = jnp.dot(
        select.astype(tile_vals.dtype),
        tile_vals.reshape(entries, tile_size * tile_size),
        preferred_element_type=jnp.float32,
    ).astype(tile_vals.dtype)
    placed = placed.reshape(tiles_per_part, tiles_per_part, tile_size, tile_size)
    side = tiles_per_part * tile_size
    return placed.transpose(0, 2, 1, 3).reshape(side, side)


def activation(pre_act, cotangent):
    logistic = jax.nn.sigmoid(pre_act)
    result = (pre_act * logistic).astype(jnp.bfloat16)
    grad_pre = (
        cotangent.astype(jnp.float32) * logistic * (1.0 + pre_act * (1.0 - logistic))
    ).astype(jnp.bfloat16)
    return (result, grad_pre)


def body(feats, weight, bias, grad_out, tile_values, tile_rows, tile_cols, tile_count):
    replicas = lax.axis_size("rep")
    rep_index = lax.axis_index("rep")
    tile_size = tile_values.shape[-1]
    pair_slots = tile_values.shape[2]
    digit_count = (replicas - 1).bit_length()
    values_here = tile_values[0, 0]
    rows_here = tile_rows[0, 0]
    cols_here = tile_cols[0, 0]
    counts_here = tile_count[0, 0]
    hw_slice = jnp.dot(feats, weight, preferred_element_type=jnp.float32).astype(jnp.bfloat16)
    feature_block = lax.all_gather(hw_slice, "rep", axis=0, tiled=True)
    for level in range(digit_count):
        shifted = passed_along(feature_block, "blk", 1 << level)
        feature_block = jnp.where(rep_index // (1 << level) % 2 == 1, shifted, feature_block)
    tiles_per_part = feature_block.shape[0] // tile_size
    adjacency = [
        dense_adjacency(
            values_here[slot], rows_here[slot], cols_here[slot], counts_here[slot], tiles_per_part
        )
        for slot in range(pair_slots)
    ]
    aggregate = jnp.zeros(feature_block.shape, jnp.float32)
    for slot in range(pair_slots):
        aggregate = aggregate + jnp.dot(
            adjacency[slot], feature_block, preferred_element_type=jnp.float32
        )
        if slot + 1 < pair_slots:
            feature_block = passed_along(feature_block, "blk", replicas)
    aggregate_rows = lax.psum_scatter(
        aggregate.astype(jnp.bfloat16), "rep", scatter_dimension=0, tiled=True
    ).astype(jnp.float32)
    out, grad_rows = activation(aggregate_rows + bias, grad_out)
    grad_block = lax.all_gather(grad_rows, "rep", axis=0, tiled=True)
    partial_grad = jnp.zeros(grad_block.shape, jnp.float32)
    for slot in reversed(range(pair_slots)):
        partial_grad = partial_grad + lax.dot_general(
            adjacency[slot],
            grad_block,
            (((0,), (0,)), ((), ())),
            preferred_element_type=jnp.float32,
        )
        if slot > 0:
            partial_grad = passed_along(partial_grad.astype(jnp.bfloat16), "blk", -replicas).astype(
                partial_grad.dtype
            )
    for level in reversed(range(digit_count)):
        shifted = passed_along(partial_grad.astype(jnp.bfloat16), "blk", -(1 << level)).astype(
            partial_grad.dtype
        )
        partial_grad = jnp.where(rep_index // (1 << level) % 2 == 1, shifted, partial_grad)
    grad_hw = lax.psum_scatter(
        partial_grad.astype(jnp.bfloat16), "rep", scatter_dimension=0, tiled=True
    )
    grad_feats = lax.dot_general(
        grad_hw, weight, (((1,), (1,)), ((), ())), preferred_element_type=jnp.float32
    ).astype(jnp.bfloat16)
    weight_terms = lax.dot_general(
        feats, grad_hw, (((0,), (0,)), ((), ())), preferred_element_type=jnp.float32
    )
    weight_rows = weight.shape[0] // replicas
    bias_terms = jnp.sum(grad_rows.astype(jnp.float32), axis=0)
    weight_total, grad_bias = lax.psum((weight_terms, bias_terms), ("blk", "rep"))
    grad_weight = lax.dynamic_slice_in_dim(weight_total, rep_index * weight_rows, weight_rows, 0)
    return (out, grad_feats, grad_weight, grad_bias)


def solution(mesh):
    in_specs = (
        P(("blk", "rep"), None),
        P(),
        P(),
        P(("blk", "rep"), None),
        P("blk", "rep", None, None, None, None),
        P("blk", "rep", None, None),
        P("blk", "rep", None, None),
        P("blk", "rep", None),
    )
    out_specs = (P(("blk", "rep"), None), P(("blk", "rep"), None), P("rep", None), P())
    return jax.shard_map(body, mesh=mesh, in_specs=in_specs, out_specs=out_specs, check_vma=False)
```

```python
import jax
import jax.numpy as jnp
from jax import lax
from jax.sharding import PartitionSpec as P


def passed_along(x, axis, by):
    devices = lax.axis_size(axis)
    return lax.ppermute(x, axis, [(i, (i + by) % devices) for i in range(devices)])


def dense_adjacency(tile_vals, tile_row, tile_col, live, tiles_per_part):
    entries, tile_size, _ = tile_vals.shape
    cells = tiles_per_part * tiles_per_part
    cell_of_entry = tile_row * tiles_per_part + tile_col
    alive = jnp.arange(entries) < live
    select = (cell_of_entry[None, :] == jnp.arange(cells)[:, None]) & alive[None, :]
    placed = jnp.dot(
        select.astype(tile_vals.dtype),
        tile_vals.reshape(entries, tile_size * tile_size),
        preferred_element_type=jnp.float32,
    ).astype(tile_vals.dtype)
    placed = placed.reshape(tiles_per_part, tiles_per_part, tile_size, tile_size)
    side = tiles_per_part * tile_size
    return placed.transpose(0, 2, 1, 3).reshape(side, side)


def activation(pre_act, cotangent):
    logistic = jax.nn.sigmoid(pre_act)
    result = (pre_act * logistic).astype(jnp.bfloat16)
    grad_pre = (
        cotangent.astype(jnp.float32) * logistic * (1.0 + pre_act * (1.0 - logistic))
    ).astype(jnp.bfloat16)
    return (result, grad_pre)


def body(feats, weight, bias, grad_out, tile_values, tile_rows, tile_cols, tile_count):
    replicas = lax.axis_size("rep")
    rep_index = lax.axis_index("rep")
    tile_size = tile_values.shape[-1]
    pair_slots = tile_values.shape[2]
    digit_count = (replicas - 1).bit_length()
    values_here = tile_values[0, 0]
    rows_here = tile_rows[0, 0]
    cols_here = tile_cols[0, 0]
    counts_here = tile_count[0, 0]
    hw_slice = jnp.dot(feats, weight, preferred_element_type=jnp.float32).astype(jnp.bfloat16)
    feature_block = lax.all_gather(hw_slice, "rep", axis=0, tiled=True)
    for level in range(digit_count):
        shifted = passed_along(feature_block, "blk", 1 << level)
        feature_block = jnp.where(rep_index // (1 << level) % 2 == 1, shifted, feature_block)
    tiles_per_part = feature_block.shape[0] // tile_size
    adjacency = [
        dense_adjacency(
            values_here[slot], rows_here[slot], cols_here[slot], counts_here[slot], tiles_per_part
        )
        for slot in range(pair_slots)
    ]
    aggregate = jnp.zeros(feature_block.shape, jnp.float32)
    for slot in range(pair_slots):
        aggregate = aggregate + jnp.dot(
            adjacency[slot], feature_block, preferred_element_type=jnp.float32
        )
        if slot + 1 < pair_slots:
            feature_block = passed_along(feature_block, "blk", replicas)
    aggregate_rows = lax.psum_scatter(
        aggregate.astype(jnp.bfloat16), "rep", scatter_dimension=0, tiled=True
    ).astype(jnp.float32)
    out, grad_rows = activation(aggregate_rows + bias, grad_out)
    grad_block = lax.all_gather(grad_rows, "rep", axis=0, tiled=True)
    partial_grad = jnp.zeros(grad_block.shape, jnp.float32)
    for slot in reversed(range(pair_slots)):
        partial_grad = partial_grad + lax.dot_general(
            adjacency[slot],
            grad_block,
            (((0,), (0,)), ((), ())),
            preferred_element_type=jnp.float32,
        )
        if slot > 0:
            partial_grad = passed_along(partial_grad.astype(jnp.bfloat16), "blk", -replicas).astype(
                partial_grad.dtype
            )
    for level in reversed(range(digit_count)):
        shifted = passed_along(partial_grad.astype(jnp.bfloat16), "blk", -(1 << level)).astype(
            partial_grad.dtype
        )
        partial_grad = jnp.where(rep_index // (1 << level) % 2 == 1, shifted, partial_grad)
    grad_hw = lax.psum_scatter(
        partial_grad.astype(jnp.bfloat16), "rep", scatter_dimension=0, tiled=True
    )
    grad_feats = lax.dot_general(
        grad_hw, weight, (((1,), (1,)), ((), ())), preferred_element_type=jnp.float32
    ).astype(jnp.bfloat16)
    weight_terms = lax.dot_general(
        feats, grad_hw, (((0,), (0,)), ((), ())), preferred_element_type=jnp.float32
    )
    weight_part = lax.psum_scatter(weight_terms, "rep", scatter_dimension=0, tiled=True)
    bias_part = jnp.sum(grad_block.astype(jnp.float32), axis=0)
    totals = lax.psum(jnp.concatenate([weight_part, bias_part[None, :]], axis=0), "blk")
    grad_weight = totals[:-1]
    grad_bias = totals[-1]
    return (out, grad_feats, grad_weight, grad_bias)


def solution(mesh):
    in_specs = (
        P(("blk", "rep"), None),
        P(),
        P(),
        P(("blk", "rep"), None),
        P("blk", "rep", None, None, None, None),
        P("blk", "rep", None, None),
        P("blk", "rep", None, None),
        P("blk", "rep", None),
    )
    out_specs = (P(("blk", "rep"), None), P(("blk", "rep"), None), P("rep", None), P())
    return jax.shard_map(body, mesh=mesh, in_specs=in_specs, out_specs=out_specs, check_vma=False)
```

```python
import jax
import jax.numpy as jnp
from jax import lax
from jax.sharding import PartitionSpec as P


def dense_adjacency(tile_vals, tile_row, tile_col, live, tiles_per_part):
    entries, tile_size, _ = tile_vals.shape
    cells = tiles_per_part * tiles_per_part
    cell_of_entry = tile_row * tiles_per_part + tile_col
    alive = jnp.arange(entries) < live
    select = (cell_of_entry[None, :] == jnp.arange(cells)[:, None]) & alive[None, :]
    placed = jnp.dot(
        select.astype(tile_vals.dtype),
        tile_vals.reshape(entries, tile_size * tile_size),
        preferred_element_type=jnp.float32,
    ).astype(tile_vals.dtype)
    placed = placed.reshape(tiles_per_part, tiles_per_part, tile_size, tile_size)
    side = tiles_per_part * tile_size
    return placed.transpose(0, 2, 1, 3).reshape(side, side)


def rep_reduce_scatter(x, wire_dtype):
    replicas = lax.axis_size("rep")
    rep_index = lax.axis_index("rep")
    bit_count = (replicas - 1).bit_length()
    rows = x.shape[0] // replicas
    current = x.reshape((2,) * bit_count + (rows,) + x.shape[1:])
    remaining = list(reversed(range(bit_count)))
    order = [0] + list(range(2, bit_count)) + [1] if bit_count > 2 else list(range(bit_count))
    for bit in order:
        axis = remaining.index(bit)
        mine = (rep_index >> bit) & 1
        keep = lax.dynamic_index_in_dim(current, mine, axis, keepdims=False)
        send = lax.dynamic_index_in_dim(current, 1 - mine, axis, keepdims=False)
        partner = [(i, i ^ (1 << bit)) for i in range(replicas)]
        got = lax.ppermute(send.astype(wire_dtype), "rep", partner)
        current = keep + got.astype(jnp.float32)
        remaining.remove(bit)
    return current


def blk_all_reduce(x):
    blocks = lax.axis_size("blk")
    step = 1
    while step < blocks:
        x = x + lax.ppermute(x, "blk", [(i, i ^ step) for i in range(blocks)])
        step <<= 1
    return x


def source_pairs(blocks, replicas, slot, half, backward):
    pairs = []
    for b in range(blocks):
        for r in range(replicas):
            src_rep = r if half == 0 else replicas - 1 - r
            src = ((b - r - slot * replicas) % blocks) * replicas + src_rep
            dst = b * replicas + r
            pairs.append((dst, src) if backward else (src, dst))
    return pairs


def activation(pre_act, cotangent):
    logistic = jax.nn.sigmoid(pre_act)
    result = (pre_act * logistic).astype(jnp.bfloat16)
    grad_pre = (
        cotangent.astype(jnp.float32) * logistic * (1.0 + pre_act * (1.0 - logistic))
    ).astype(jnp.bfloat16)
    return (result, grad_pre)


def body(feats, weight, bias, grad_out, tile_values, tile_rows, tile_cols, tile_count):
    replicas = lax.axis_size("rep")
    blocks = lax.axis_size("blk")
    tile_size = tile_values.shape[-1]
    pair_slots = tile_values.shape[2]
    values_here = tile_values[0, 0]
    rows_here = tile_rows[0, 0]
    cols_here = tile_cols[0, 0]
    counts_here = tile_count[0, 0]
    hw_slice = jnp.dot(feats, weight, preferred_element_type=jnp.float32).astype(jnp.bfloat16)
    partition = lax.all_gather(hw_slice, "rep", axis=0, tiled=True)
    part_rows = partition.shape[0]
    half_rows = part_rows // 2
    tiles_per_part = part_rows // tile_size
    both_axes = ("blk", "rep")
    sources = []
    for slot in range(pair_slots):
        halves = [
            lax.ppermute(
                partition[half * half_rows:(half + 1) * half_rows],
                both_axes,
                source_pairs(blocks, replicas, slot, half, False),
            )
            for half in range(2)
        ]
        sources.append(jnp.concatenate(halves, axis=0))
    adjacency = [
        dense_adjacency(
            values_here[slot], rows_here[slot], cols_here[slot], counts_here[slot], tiles_per_part
        )
        for slot in range(pair_slots)
    ]
    aggregate = jnp.zeros(partition.shape, jnp.float32)
    for slot in range(pair_slots):
        aggregate = aggregate + jnp.dot(
            adjacency[slot], sources[slot], preferred_element_type=jnp.float32
        )
    aggregate_rows = rep_reduce_scatter(aggregate, jnp.bfloat16)
    out, grad_rows = activation(aggregate_rows + bias, grad_out)
    grad_block = lax.all_gather(grad_rows, "rep", axis=0, tiled=True)
    returned = [jnp.zeros((half_rows, partition.shape[1]), jnp.float32) for _ in range(2)]
    for slot in range(pair_slots):
        partial = lax.dot_general(
            adjacency[slot],
            grad_block,
            (((0,), (0,)), ((), ())),
            preferred_element_type=jnp.float32,
        ).astype(jnp.bfloat16)
        for half in range(2):
            got = lax.ppermute(
                partial[half * half_rows:(half + 1) * half_rows],
                both_axes,
                source_pairs(blocks, replicas, slot, half, True),
            )
            returned[half] = returned[half] + got.astype(jnp.float32)
    partial_grad = jnp.concatenate(returned, axis=0)
    grad_hw = rep_reduce_scatter(partial_grad, jnp.bfloat16).astype(jnp.bfloat16)
    grad_feats = lax.dot_general(
        grad_hw, weight, (((1,), (1,)), ((), ())), preferred_element_type=jnp.float32
    ).astype(jnp.bfloat16)
    weight_terms = lax.dot_general(
        feats, grad_hw, (((0,), (0,)), ((), ())), preferred_element_type=jnp.float32
    )
    weight_part = rep_reduce_scatter(weight_terms, jnp.float32)
    bias_part = jnp.sum(grad_block.astype(jnp.float32), axis=0)
    totals = blk_all_reduce(jnp.concatenate([weight_part, bias_part[None, :]], axis=0))
    grad_weight = totals[:-1]
    grad_bias = totals[-1]
    return (out, grad_feats, grad_weight, grad_bias)


def solution(mesh):
    in_specs = (
        P(("blk", "rep"), None),
        P(),
        P(),
        P(("blk", "rep"), None),
        P("blk", "rep", None, None, None, None),
        P("blk", "rep", None, None),
        P("blk", "rep", None, None),
        P("blk", "rep", None),
    )
    out_specs = (P(("blk", "rep"), None), P(("blk", "rep"), None), P("rep", None), P())
    return jax.shard_map(body, mesh=mesh, in_specs=in_specs, out_specs=out_specs, check_vma=False)
```

```python
import jax
import jax.numpy as jnp
from jax import lax
from jax.sharding import PartitionSpec as P


def dense_adjacency(tile_vals, tile_row, tile_col, live, tiles_per_part):
    entries, tile_size, _ = tile_vals.shape
    cells = tiles_per_part * tiles_per_part
    cell_of_entry = tile_row * tiles_per_part + tile_col
    alive = jnp.arange(entries) < live
    select = (cell_of_entry[None, :] == jnp.arange(cells)[:, None]) & alive[None, :]
    placed = jnp.dot(
        select.astype(tile_vals.dtype),
        tile_vals.reshape(entries, tile_size * tile_size),
        preferred_element_type=jnp.float32,
    ).astype(tile_vals.dtype)
    placed = placed.reshape(tiles_per_part, tiles_per_part, tile_size, tile_size)
    side = tiles_per_part * tile_size
    return placed.transpose(0, 2, 1, 3).reshape(side, side)


def rep_reduce_scatter(x, wire_dtype):
    replicas = lax.axis_size("rep")
    rep_index = lax.axis_index("rep")
    bit_count = (replicas - 1).bit_length()
    rows = x.shape[0] // replicas
    current = x.reshape((2,) * bit_count + (rows,) + x.shape[1:])
    remaining = list(reversed(range(bit_count)))
    order = [0] + list(range(2, bit_count)) + [1] if bit_count > 2 else list(range(bit_count))
    for bit in order:
        axis = remaining.index(bit)
        mine = (rep_index >> bit) & 1
        keep = lax.dynamic_index_in_dim(current, mine, axis, keepdims=False)
        send = lax.dynamic_index_in_dim(current, 1 - mine, axis, keepdims=False)
        partner = [(i, i ^ (1 << bit)) for i in range(replicas)]
        got = lax.ppermute(send.astype(wire_dtype), "rep", partner)
        current = keep + got.astype(jnp.float32)
        remaining.remove(bit)
    return current


def blk_all_reduce(x):
    blocks = lax.axis_size("blk")
    step = 1
    while step < blocks:
        x = x + lax.ppermute(x, "blk", [(i, i ^ step) for i in range(blocks)])
        step <<= 1
    return x


def source_pairs(blocks, replicas, slot, half, backward):
    pairs = []
    for b in range(blocks):
        for r in range(replicas):
            src_rep = r if half == 0 else replicas - 1 - r
            src = ((b - r - slot * replicas) % blocks) * replicas + src_rep
            dst = b * replicas + r
            pairs.append((dst, src) if backward else (src, dst))
    return pairs


def activation(pre_act, cotangent):
    logistic = jax.nn.sigmoid(pre_act)
    result = (pre_act * logistic).astype(jnp.bfloat16)
    grad_pre = (
        cotangent.astype(jnp.float32) * logistic * (1.0 + pre_act * (1.0 - logistic))
    ).astype(jnp.bfloat16)
    return (result, grad_pre)


def body(feats, weight, bias, grad_out, tile_values, tile_rows, tile_cols, tile_count):
    replicas = lax.axis_size("rep")
    blocks = lax.axis_size("blk")
    tile_size = tile_values.shape[-1]
    pair_slots = tile_values.shape[2]
    values_here = tile_values[0, 0]
    rows_here = tile_rows[0, 0]
    cols_here = tile_cols[0, 0]
    counts_here = tile_count[0, 0]
    partition = lax.all_gather(feats, "rep", axis=0, tiled=True)
    part_rows = partition.shape[0]
    half_rows = part_rows // 2
    tiles_per_part = part_rows // tile_size
    both_axes = ("blk", "rep")
    sources = []
    for slot in range(pair_slots):
        halves = [
            lax.ppermute(
                partition[half * half_rows:(half + 1) * half_rows],
                both_axes,
                source_pairs(blocks, replicas, slot, half, False),
            )
            for half in range(2)
        ]
        sources.append(jnp.concatenate(halves, axis=0))
    adjacency = [
        dense_adjacency(
            values_here[slot], rows_here[slot], cols_here[slot], counts_here[slot], tiles_per_part
        )
        for slot in range(pair_slots)
    ]
    aggregated_feats = jnp.zeros(partition.shape, jnp.float32)
    for slot in range(pair_slots):
        aggregated_feats = aggregated_feats + jnp.dot(
            adjacency[slot], sources[slot], preferred_element_type=jnp.float32
        )
    aggregate = jnp.dot(
        aggregated_feats,
        weight.astype(jnp.float32),
        precision=lax.Precision.HIGHEST,
        preferred_element_type=jnp.float32,
    )
    aggregate_rows = rep_reduce_scatter(aggregate, jnp.bfloat16)
    out, grad_rows = activation(aggregate_rows + bias, grad_out)
    grad_block = lax.all_gather(grad_rows, "rep", axis=0, tiled=True)
    weight_terms = lax.dot_general(
        aggregated_feats,
        grad_block.astype(jnp.float32),
        (((0,), (0,)), ((), ())),
        precision=lax.Precision.HIGHEST,
        preferred_element_type=jnp.float32,
    )
    weight_part = rep_reduce_scatter(weight_terms, jnp.float32)
    bias_part = jnp.sum(grad_block.astype(jnp.float32), axis=0)
    totals = blk_all_reduce(jnp.concatenate([weight_part, bias_part[None, :]], axis=0))
    returned = [jnp.zeros((half_rows, partition.shape[1]), jnp.float32) for _ in range(2)]
    for slot in range(pair_slots):
        partial = lax.dot_general(
            adjacency[slot],
            grad_block,
            (((0,), (0,)), ((), ())),
            preferred_element_type=jnp.float32,
        ).astype(jnp.bfloat16)
        for half in range(2):
            got = lax.ppermute(
                partial[half * half_rows:(half + 1) * half_rows],
                both_axes,
                source_pairs(blocks, replicas, slot, half, True),
            )
            returned[half] = returned[half] + got.astype(jnp.float32)
    partial_grad = jnp.concatenate(returned, axis=0)
    grad_hw = rep_reduce_scatter(partial_grad, jnp.bfloat16).astype(jnp.bfloat16)
    grad_feats = lax.dot_general(
        grad_hw, weight, (((1,), (1,)), ((), ())), preferred_element_type=jnp.float32
    ).astype(jnp.bfloat16)
    grad_weight = totals[:-1]
    grad_bias = totals[-1]
    return (out, grad_feats, grad_weight, grad_bias)


def solution(mesh):
    in_specs = (
        P(("blk", "rep"), None),
        P(),
        P(),
        P(("blk", "rep"), None),
        P("blk", "rep", None, None, None, None),
        P("blk", "rep", None, None),
        P("blk", "rep", None, None),
        P("blk", "rep", None),
    )
    out_specs = (P(("blk", "rep"), None), P(("blk", "rep"), None), P("rep", None), P())
    return jax.shard_map(body, mesh=mesh, in_specs=in_specs, out_specs=out_specs, check_vma=False)
```

```python
import jax
import jax.numpy as jnp
from jax import lax
from jax.sharding import PartitionSpec as P


def dense_adjacency(tile_vals, tile_row, tile_col, live, tiles_per_part):
    entries, tile_size, _ = tile_vals.shape
    cells = tiles_per_part * tiles_per_part
    cell_of_entry = tile_row * tiles_per_part + tile_col
    alive = jnp.arange(entries) < live
    select = (cell_of_entry[None, :] == jnp.arange(cells)[:, None]) & alive[None, :]
    placed = jnp.dot(
        select.astype(tile_vals.dtype),
        tile_vals.reshape(entries, tile_size * tile_size),
        preferred_element_type=jnp.float32,
    ).astype(tile_vals.dtype)
    placed = placed.reshape(tiles_per_part, tiles_per_part, tile_size, tile_size)
    side = tiles_per_part * tile_size
    return placed.transpose(0, 2, 1, 3).reshape(side, side)


def rep_reduce_scatter(x, wire_dtype):
    replicas = lax.axis_size("rep")
    rep_index = lax.axis_index("rep")
    bit_count = (replicas - 1).bit_length()
    rows = x.shape[0] // replicas
    current = x.reshape((2,) * bit_count + (rows,) + x.shape[1:])
    remaining = list(reversed(range(bit_count)))
    order = [0] + list(range(2, bit_count)) + [1] if bit_count > 2 else list(range(bit_count))
    for bit in order:
        axis = remaining.index(bit)
        mine = (rep_index >> bit) & 1
        keep = lax.dynamic_index_in_dim(current, mine, axis, keepdims=False)
        send = lax.dynamic_index_in_dim(current, 1 - mine, axis, keepdims=False)
        partner = [(i, i ^ (1 << bit)) for i in range(replicas)]
        got = lax.ppermute(send.astype(wire_dtype), "rep", partner)
        current = keep + got.astype(jnp.float32)
        remaining.remove(bit)
    return current


def blk_all_reduce(x):
    blocks = lax.axis_size("blk")
    step = 1
    while step < blocks:
        x = x + lax.ppermute(x, "blk", [(i, i ^ step) for i in range(blocks)])
        step <<= 1
    return x


def source_pairs(blocks, replicas, slot, half, backward):
    pairs = []
    for b in range(blocks):
        for r in range(replicas):
            src_rep = r if half == 0 else replicas - 1 - r
            src = ((b - r - slot * replicas) % blocks) * replicas + src_rep
            dst = b * replicas + r
            pairs.append((dst, src) if backward else (src, dst))
    return pairs


def activation(pre_act, cotangent):
    logistic = jax.nn.sigmoid(pre_act)
    result = (pre_act * logistic).astype(jnp.bfloat16)
    grad_pre = (
        cotangent.astype(jnp.float32) * logistic * (1.0 + pre_act * (1.0 - logistic))
    ).astype(jnp.bfloat16)
    return (result, grad_pre)


def body(feats, weight, bias, grad_out, tile_values, tile_rows, tile_cols, tile_count):
    replicas = lax.axis_size("rep")
    blocks = lax.axis_size("blk")
    tile_size = tile_values.shape[-1]
    pair_slots = tile_values.shape[2]
    values_here = tile_values[0, 0]
    rows_here = tile_rows[0, 0]
    cols_here = tile_cols[0, 0]
    counts_here = tile_count[0, 0]
    partition = lax.all_gather(feats, "rep", axis=0, tiled=True)
    part_rows = partition.shape[0]
    half_rows = part_rows // 2
    tiles_per_part = part_rows // tile_size
    both_axes = ("blk", "rep")
    sources = []
    for slot in range(pair_slots):
        halves = [
            lax.ppermute(
                partition[half * half_rows:(half + 1) * half_rows],
                both_axes,
                source_pairs(blocks, replicas, slot, half, False),
            )
            for half in range(2)
        ]
        sources.append(jnp.concatenate(halves, axis=0))
    adjacency = [
        dense_adjacency(
            values_here[slot], rows_here[slot], cols_here[slot], counts_here[slot], tiles_per_part
        )
        for slot in range(pair_slots)
    ]
    aggregated_feats = jnp.zeros(partition.shape, jnp.float32)
    for slot in range(pair_slots):
        aggregated_feats = aggregated_feats + jnp.dot(
            adjacency[slot], sources[slot], preferred_element_type=jnp.float32
        )
    aggregate = jnp.dot(
        aggregated_feats,
        weight.astype(jnp.float32),
        precision=lax.Precision.HIGHEST,
        preferred_element_type=jnp.float32,
    )
    aggregate_rows = rep_reduce_scatter(aggregate, jnp.bfloat16)
    out, grad_rows = activation(aggregate_rows + bias, grad_out)
    grad_block = lax.all_gather(grad_rows, "rep", axis=0, tiled=True)
    weight_terms = lax.dot_general(
        aggregated_feats,
        grad_block.astype(jnp.float32),
        (((0,), (0,)), ((), ())),
        precision=lax.Precision.HIGHEST,
        preferred_element_type=jnp.float32,
    )
    weight_part = rep_reduce_scatter(weight_terms, jnp.float32)
    bias_part = jnp.sum(grad_block.astype(jnp.float32), axis=0)
    totals = blk_all_reduce(jnp.concatenate([weight_part, bias_part[None, :]], axis=0))
    arrived = []
    for slot in range(pair_slots):
        partial = lax.dot_general(
            adjacency[slot],
            grad_block,
            (((0,), (0,)), ((), ())),
            preferred_element_type=jnp.float32,
        ).astype(jnp.bfloat16)
        for half in range(2):
            arrived.append(
                lax.ppermute(
                    partial[half * half_rows:(half + 1) * half_rows],
                    both_axes,
                    source_pairs(blocks, replicas, slot, half, True),
                )
            )
    arrived, totals = lax.optimization_barrier((arrived, totals))
    returned = [jnp.zeros((half_rows, partition.shape[1]), jnp.float32) for _ in range(2)]
    for index, got in enumerate(arrived):
        returned[index % 2] = returned[index % 2] + got.astype(jnp.float32)
    partial_grad = jnp.concatenate(returned, axis=0)
    grad_hw = rep_reduce_scatter(partial_grad, jnp.bfloat16).astype(jnp.bfloat16)
    grad_feats = lax.dot_general(
        grad_hw, weight, (((1,), (1,)), ((), ())), preferred_element_type=jnp.float32
    ).astype(jnp.bfloat16)
    grad_weight = totals[:-1]
    grad_bias = totals[-1]
    return (out, grad_feats, grad_weight, grad_bias)


def solution(mesh):
    in_specs = (
        P(("blk", "rep"), None),
        P(),
        P(),
        P(("blk", "rep"), None),
        P("blk", "rep", None, None, None, None),
        P("blk", "rep", None, None),
        P("blk", "rep", None, None),
        P("blk", "rep", None),
    )
    out_specs = (P(("blk", "rep"), None), P(("blk", "rep"), None), P("rep", None), P())
    return jax.shard_map(body, mesh=mesh, in_specs=in_specs, out_specs=out_specs, check_vma=False)
```

```python
import jax
import jax.numpy as jnp
from jax import lax
from jax.sharding import PartitionSpec as P


def dense_adjacency(tile_vals, tile_row, tile_col, live, tiles_per_part):
    entries, tile_size, _ = tile_vals.shape
    cells = tiles_per_part * tiles_per_part
    cell_of_entry = tile_row * tiles_per_part + tile_col
    alive = jnp.arange(entries) < live
    select = (cell_of_entry[None, :] == jnp.arange(cells)[:, None]) & alive[None, :]
    placed = jnp.dot(
        select.astype(tile_vals.dtype),
        tile_vals.reshape(entries, tile_size * tile_size),
        preferred_element_type=jnp.float32,
    ).astype(tile_vals.dtype)
    placed = placed.reshape(tiles_per_part, tiles_per_part, tile_size, tile_size)
    side = tiles_per_part * tile_size
    return placed.transpose(0, 2, 1, 3).reshape(side, side)


def rep_reduce_scatter(x, wire_dtype, order):
    replicas = lax.axis_size("rep")
    rep_index = lax.axis_index("rep")
    rows = x.shape[0] >> len(order)
    current = x.reshape((2,) * len(order) + (rows,) + x.shape[1:])
    remaining = sorted(order, reverse=True)
    for bit in order:
        axis = remaining.index(bit)
        mine = (rep_index >> bit) & 1
        keep = lax.dynamic_index_in_dim(current, mine, axis, keepdims=False)
        send = lax.dynamic_index_in_dim(current, 1 - mine, axis, keepdims=False)
        partner = [(i, i ^ (1 << bit)) for i in range(replicas)]
        got = lax.ppermute(send.astype(wire_dtype), "rep", partner)
        current = keep + got.astype(jnp.float32)
        remaining.remove(bit)
    return current


def rep_all_gather(x, order):
    replicas = lax.axis_size("rep")
    rep_index = lax.axis_index("rep")
    current = x
    held = []
    for bit in order:
        partner = [(i, i ^ (1 << bit)) for i in range(replicas)]
        got = lax.ppermute(current, "rep", partner)
        upper = ((rep_index >> bit) & 1) == 1
        low = jnp.where(upper, got, current)
        high = jnp.where(upper, current, got)
        held = sorted(held + [bit], reverse=True)
        current = jnp.stack([low, high], axis=held.index(bit))
    return current.reshape((-1,) + x.shape[1:])


def blk_all_reduce(x):
    blocks = lax.axis_size("blk")
    step = 1
    while step < blocks:
        x = x + lax.ppermute(x, "blk", [(i, i ^ step) for i in range(blocks)])
        step <<= 1
    return x


def route_target(source_rep, route, replicas):
    half = replicas // 2
    if route == 0:
        return source_rep if source_rep < half else replicas + half - 1 - source_rep
    return replicas - 1 - source_rep if source_rep < half else source_rep - half


def route_pairs(blocks, replicas, slot, route, backward):
    pairs = []
    for b in range(blocks):
        for s in range(replicas):
            d = route_target(s, route, replicas)
            src = b * replicas + s
            dst = ((b + d + slot * replicas) % blocks) * replicas + d
            pairs.append((dst, src) if backward else (src, dst))
    return pairs


def activation(pre_act, cotangent):
    logistic = jax.nn.sigmoid(pre_act)
    result = (pre_act * logistic).astype(jnp.bfloat16)
    grad_pre = (
        cotangent.astype(jnp.float32) * logistic * (1.0 + pre_act * (1.0 - logistic))
    ).astype(jnp.bfloat16)
    return (result, grad_pre)


def body(feats, weight, bias, grad_out, tile_values, tile_rows, tile_cols, tile_count):
    replicas = lax.axis_size("rep")
    blocks = lax.axis_size("blk")
    tile_size = tile_values.shape[-1]
    pair_slots = tile_values.shape[2]
    values_here = tile_values[0, 0]
    rows_here = tile_rows[0, 0]
    cols_here = tile_cols[0, 0]
    counts_here = tile_count[0, 0]
    replica_bits = (replicas - 1).bit_length()
    gather_bits = [1] + list(range(2, replica_bits - 1)) + [0]
    held_half = rep_all_gather(feats, gather_bits)
    half_rows = held_half.shape[0]
    part_rows = 2 * half_rows
    tiles_per_part = part_rows // tile_size
    both_axes = ("blk", "rep")
    upper_rep = lax.axis_index("rep") >= replicas // 2
    sources = []
    for slot in range(pair_slots):
        by_route = [
            lax.ppermute(held_half, both_axes, route_pairs(blocks, replicas, slot, route, False))
            for route in range(2)
        ]
        sources.append(
            jnp.where(
                upper_rep,
                jnp.concatenate([by_route[1], by_route[0]], axis=0),
                jnp.concatenate([by_route[0], by_route[1]], axis=0),
            )
        )
    adjacency = [
        dense_adjacency(
            values_here[slot], rows_here[slot], cols_here[slot], counts_here[slot], tiles_per_part
        )
        for slot in range(pair_slots)
    ]
    aggregated_feats = jnp.zeros((part_rows, feats.shape[1]), jnp.float32)
    for slot in range(pair_slots):
        aggregated_feats = aggregated_feats + jnp.dot(
            adjacency[slot], sources[slot], preferred_element_type=jnp.float32
        )
    aggregate = jnp.dot(
        aggregated_feats,
        weight.astype(jnp.float32),
        precision=lax.Precision.HIGHEST,
        preferred_element_type=jnp.float32,
    )
    full_bits = [0] + list(range(2, replica_bits)) + [1]
    aggregate_rows = rep_reduce_scatter(aggregate, jnp.bfloat16, full_bits)
    out, grad_rows = activation(aggregate_rows + bias, grad_out)
    grad_block = lax.all_gather(grad_rows, "rep", axis=0, tiled=True)
    weight_terms = lax.dot_general(
        aggregated_feats,
        grad_block.astype(jnp.float32),
        (((0,), (0,)), ((), ())),
        precision=lax.Precision.HIGHEST,
        preferred_element_type=jnp.float32,
    )
    weight_part = rep_reduce_scatter(weight_terms, jnp.float32, full_bits)
    bias_part = jnp.sum(grad_block.astype(jnp.float32), axis=0)
    totals = blk_all_reduce(jnp.concatenate([weight_part, bias_part[None, :]], axis=0))
    returned = jnp.zeros((half_rows, feats.shape[1]), jnp.float32)
    for slot in range(pair_slots):
        partial = lax.dot_general(
            adjacency[slot],
            grad_block,
            (((0,), (0,)), ((), ())),
            preferred_element_type=jnp.float32,
        ).astype(jnp.bfloat16)
        first, second = partial[:half_rows], partial[half_rows:]
        for route in range(2):
            own_half = jnp.where(upper_rep, second, first)
            other_half = jnp.where(upper_rep, first, second)
            got = lax.ppermute(
                own_half if route == 0 else other_half,
                both_axes,
                route_pairs(blocks, replicas, slot, route, True),
            )
            returned = returned + got.astype(jnp.float32)
    half_bits = [0] + list(range(2, replica_bits - 1)) + [1]
    grad_hw = rep_reduce_scatter(returned, jnp.bfloat16, half_bits).astype(jnp.bfloat16)
    grad_feats = lax.dot_general(
        grad_hw, weight, (((1,), (1,)), ((), ())), preferred_element_type=jnp.float32
    ).astype(jnp.bfloat16)
    grad_weight = totals[:-1]
    grad_bias = totals[-1]
    return (out, grad_feats, grad_weight, grad_bias)


def solution(mesh):
    in_specs = (
        P(("blk", "rep"), None),
        P(),
        P(),
        P(("blk", "rep"), None),
        P("blk", "rep", None, None, None, None),
        P("blk", "rep", None, None),
        P("blk", "rep", None, None),
        P("blk", "rep", None),
    )
    out_specs = (P(("blk", "rep"), None), P(("blk", "rep"), None), P("rep", None), P())
    return jax.shard_map(body, mesh=mesh, in_specs=in_specs, out_specs=out_specs, check_vma=False)
```

```python
import jax
import jax.numpy as jnp
from jax import lax
from jax.sharding import PartitionSpec as P


def dense_adjacency(tile_vals, tile_row, tile_col, live, tiles_per_part):
    entries, tile_size, _ = tile_vals.shape
    cells = tiles_per_part * tiles_per_part
    cell_of_entry = tile_row * tiles_per_part + tile_col
    alive = jnp.arange(entries) < live
    select = (cell_of_entry[None, :] == jnp.arange(cells)[:, None]) & alive[None, :]
    placed = jnp.dot(
        select.astype(tile_vals.dtype),
        tile_vals.reshape(entries, tile_size * tile_size),
        preferred_element_type=jnp.float32,
    ).astype(tile_vals.dtype)
    placed = placed.reshape(tiles_per_part, tiles_per_part, tile_size, tile_size)
    side = tiles_per_part * tile_size
    return placed.transpose(0, 2, 1, 3).reshape(side, side)


def index_bits(current, remaining, bits, values):
    for bit, value in sorted(zip(bits, values), key=lambda pair: remaining.index(pair[0]), reverse=True):
        current = lax.dynamic_index_in_dim(current, value, remaining.index(bit), keepdims=False)
    return current


def rep_reduce_scatter(x, wire_dtype, groups):
    replicas = lax.axis_size("rep")
    rep_index = lax.axis_index("rep")
    bit_count = (replicas - 1).bit_length()
    rows = x.shape[0] // replicas
    current = x.reshape((2,) * bit_count + (rows,) + x.shape[1:])
    remaining = list(reversed(range(bit_count)))
    for bits in groups:
        mine = [(rep_index >> bit) & 1 for bit in bits]
        total = index_bits(current, remaining, bits, mine)
        for offset in range(1, 1 << len(bits)):
            flips = [(offset >> k) & 1 for k in range(len(bits))]
            mask = sum(flip << bit for flip, bit in zip(flips, bits))
            send = index_bits(current, remaining, bits, [m ^ f for m, f in zip(mine, flips)])
            got = lax.ppermute(send.astype(wire_dtype), "rep", [(i, i ^ mask) for i in range(replicas)])
            total = total + got.astype(jnp.float32)
        current = total
        remaining = [bit for bit in remaining if bit not in bits]
    return current


def blk_all_reduce(x, groups):
    blocks = lax.axis_size("blk")
    blk_index = lax.axis_index("blk")
    for bits in groups:
        members = 1 << len(bits)
        mine = sum(((blk_index >> bit) & 1) << k for k, bit in enumerate(bits))
        by_offset = [x]
        for offset in range(1, members):
            mask = sum(((offset >> k) & 1) << bit for k, bit in enumerate(bits))
            by_offset.append(lax.ppermute(x, "blk", [(i, i ^ mask) for i in range(blocks)]))
        stacked = jnp.stack(by_offset)
        ordered = jnp.take(stacked, jnp.arange(members) ^ mine, axis=0)
        x = ordered[0]
        for member in range(1, members):
            x = x + ordered[member]
    return x


def source_pairs(blocks, replicas, slot, half, backward):
    pairs = []
    for b in range(blocks):
        for r in range(replicas):
            src_rep = r if half == 0 else replicas - 1 - r
            src = ((b - r - slot * replicas) % blocks) * replicas + src_rep
            dst = b * replicas + r
            pairs.append((dst, src) if backward else (src, dst))
    return pairs


def activation(pre_act, cotangent):
    logistic = jax.nn.sigmoid(pre_act)
    result = (pre_act * logistic).astype(jnp.bfloat16)
    grad_pre = (
        cotangent.astype(jnp.float32) * logistic * (1.0 + pre_act * (1.0 - logistic))
    ).astype(jnp.bfloat16)
    return (result, grad_pre)


def body(feats, weight, bias, grad_out, tile_values, tile_rows, tile_cols, tile_count):
    replicas = lax.axis_size("rep")
    blocks = lax.axis_size("blk")
    tile_size = tile_values.shape[-1]
    pair_slots = tile_values.shape[2]
    values_here = tile_values[0, 0]
    rows_here = tile_rows[0, 0]
    cols_here = tile_cols[0, 0]
    counts_here = tile_count[0, 0]
    partition = lax.all_gather(feats, "rep", axis=0, tiled=True)
    part_rows = partition.shape[0]
    half_rows = part_rows // 2
    tiles_per_part = part_rows // tile_size
    both_axes = ("blk", "rep")
    sources = []
    for slot in range(pair_slots):
        halves = [
            lax.ppermute(
                partition[half * half_rows:(half + 1) * half_rows],
                both_axes,
                source_pairs(blocks, replicas, slot, half, False),
            )
            for half in range(2)
        ]
        sources.append(jnp.concatenate(halves, axis=0))
    adjacency = [
        dense_adjacency(
            values_here[slot], rows_here[slot], cols_here[slot], counts_here[slot], tiles_per_part
        )
        for slot in range(pair_slots)
    ]
    aggregated_feats = jnp.zeros(partition.shape, jnp.float32)
    for slot in range(pair_slots):
        aggregated_feats = aggregated_feats + jnp.dot(
            adjacency[slot], sources[slot], preferred_element_type=jnp.float32
        )
    aggregate = jnp.dot(
        aggregated_feats,
        weight.astype(jnp.float32),
        precision=lax.Precision.HIGHEST,
        preferred_element_type=jnp.float32,
    )
    rep_groups = [[0, 2], [3, 1]]
    aggregate_rows = rep_reduce_scatter(aggregate, jnp.bfloat16, rep_groups)
    out, grad_rows = activation(aggregate_rows + bias, grad_out)
    grad_block = lax.all_gather(grad_rows, "rep", axis=0, tiled=True)
    weight_terms = lax.dot_general(
        aggregated_feats,
        grad_block.astype(jnp.float32),
        (((0,), (0,)), ((), ())),
        precision=lax.Precision.HIGHEST,
        preferred_element_type=jnp.float32,
    )
    weight_part = rep_reduce_scatter(weight_terms, jnp.float32, rep_groups)
    bias_part = jnp.sum(grad_block.astype(jnp.float32), axis=0)
    totals = blk_all_reduce(
        jnp.concatenate([weight_part, bias_part[None, :]], axis=0), [[0, 1], [2, 3, 4]]
    )
    returned = [jnp.zeros((half_rows, partition.shape[1]), jnp.float32) for _ in range(2)]
    for slot in range(pair_slots):
        partial = lax.dot_general(
            adjacency[slot],
            grad_block,
            (((0,), (0,)), ((), ())),
            preferred_element_type=jnp.float32,
        ).astype(jnp.bfloat16)
        for half in range(2):
            got = lax.ppermute(
                partial[half * half_rows:(half + 1) * half_rows],
                both_axes,
                source_pairs(blocks, replicas, slot, half, True),
            )
            returned[half] = returned[half] + got.astype(jnp.float32)
    partial_grad = jnp.concatenate(returned, axis=0)
    grad_hw = rep_reduce_scatter(partial_grad, jnp.bfloat16, rep_groups).astype(jnp.bfloat16)
    grad_feats = lax.dot_general(
        grad_hw, weight, (((1,), (1,)), ((), ())), preferred_element_type=jnp.float32
    ).astype(jnp.bfloat16)
    grad_weight = totals[:-1]
    grad_bias = totals[-1]
    return (out, grad_feats, grad_weight, grad_bias)


def solution(mesh):
    in_specs = (
        P(("blk", "rep"), None),
        P(),
        P(),
        P(("blk", "rep"), None),
        P("blk", "rep", None, None, None, None),
        P("blk", "rep", None, None),
        P("blk", "rep", None, None),
        P("blk", "rep", None),
    )
    out_specs = (P(("blk", "rep"), None), P(("blk", "rep"), None), P("rep", None), P())
    return jax.shard_map(body, mesh=mesh, in_specs=in_specs, out_specs=out_specs, check_vma=False)
```

```python
import jax
import jax.numpy as jnp
from jax import lax
from jax.sharding import PartitionSpec as P


def dense_adjacency(tile_vals, tile_row, tile_col, live, tiles_per_part):
    entries, tile_size, _ = tile_vals.shape
    cells = tiles_per_part * tiles_per_part
    cell_of_entry = tile_row * tiles_per_part + tile_col
    alive = jnp.arange(entries) < live
    select = (cell_of_entry[None, :] == jnp.arange(cells)[:, None]) & alive[None, :]
    placed = jnp.dot(
        select.astype(tile_vals.dtype),
        tile_vals.reshape(entries, tile_size * tile_size),
        preferred_element_type=jnp.float32,
    ).astype(tile_vals.dtype)
    placed = placed.reshape(tiles_per_part, tiles_per_part, tile_size, tile_size)
    side = tiles_per_part * tile_size
    return placed.transpose(0, 2, 1, 3).reshape(side, side)


def rep_reduce_scatter(x, wire_dtype):
    replicas = lax.axis_size("rep")
    rep_index = lax.axis_index("rep")
    bit_count = (replicas - 1).bit_length()
    rows = x.shape[0] // replicas
    current = x.reshape((2,) * bit_count + (rows,) + x.shape[1:])
    remaining = list(reversed(range(bit_count)))
    order = [0] + list(range(2, bit_count)) + [1] if bit_count > 2 else list(range(bit_count))
    for bit in order:
        axis = remaining.index(bit)
        mine = (rep_index >> bit) & 1
        keep = lax.dynamic_index_in_dim(current, mine, axis, keepdims=False)
        send = lax.dynamic_index_in_dim(current, 1 - mine, axis, keepdims=False)
        partner = [(i, i ^ (1 << bit)) for i in range(replicas)]
        got = lax.ppermute(send.astype(wire_dtype), "rep", partner)
        current = keep + got.astype(jnp.float32)
        remaining.remove(bit)
    return current


def blk_all_reduce(x):
    blocks = lax.axis_size("blk")
    step = 1
    while step < blocks:
        x = x + lax.ppermute(x, "blk", [(i, i ^ step) for i in range(blocks)])
        step <<= 1
    return x


def source_pairs(blocks, replicas, slot, half, backward):
    pairs = []
    for b in range(blocks):
        for r in range(replicas):
            src_rep = r if half == 0 else replicas - 1 - r
            src = ((b - r - slot * replicas) % blocks) * replicas + src_rep
            dst = b * replicas + r
            pairs.append((dst, src) if backward else (src, dst))
    return pairs


def activation(pre_act, cotangent):
    logistic = jax.nn.sigmoid(pre_act)
    result = (pre_act * logistic).astype(jnp.bfloat16)
    grad_pre = (
        cotangent.astype(jnp.float32) * logistic * (1.0 + pre_act * (1.0 - logistic))
    ).astype(jnp.bfloat16)
    return (result, grad_pre)


def body(feats, weight, bias, grad_out, tile_values, tile_rows, tile_cols, tile_count):
    replicas = lax.axis_size("rep")
    blocks = lax.axis_size("blk")
    tile_size = tile_values.shape[-1]
    pair_slots = tile_values.shape[2]
    values_here = tile_values[0, 0]
    rows_here = tile_rows[0, 0]
    cols_here = tile_cols[0, 0]
    counts_here = tile_count[0, 0]
    partition = lax.all_gather(feats, "rep", axis=0, tiled=True)
    part_rows = partition.shape[0]
    half_rows = part_rows // 2
    tiles_per_part = part_rows // tile_size
    both_axes = ("blk", "rep")
    sources = []
    for slot in range(pair_slots):
        halves = [
            lax.ppermute(
                partition[half * half_rows:(half + 1) * half_rows],
                both_axes,
                source_pairs(blocks, replicas, slot, half, False),
            )
            for half in range(2)
        ]
        sources.append(jnp.concatenate(halves, axis=0))
    adjacency = [
        dense_adjacency(
            values_here[slot], rows_here[slot], cols_here[slot], counts_here[slot], tiles_per_part
        )
        for slot in range(pair_slots)
    ]
    aggregated_feats = jnp.zeros(partition.shape, jnp.float32)
    for slot in range(pair_slots):
        aggregated_feats = aggregated_feats + jnp.dot(
            adjacency[slot], sources[slot], preferred_element_type=jnp.float32
        )
    aggregate = jnp.dot(
        aggregated_feats,
        weight.astype(jnp.float32),
        precision=lax.Precision.HIGHEST,
        preferred_element_type=jnp.float32,
    )
    aggregate_rows = rep_reduce_scatter(aggregate, jnp.bfloat16)
    out, grad_rows = activation(aggregate_rows + bias, grad_out)
    grad_block = lax.all_gather(grad_rows, "rep", axis=0, tiled=True)
    weight_terms = lax.dot_general(
        aggregated_feats,
        grad_block.astype(jnp.float32),
        (((0,), (0,)), ((), ())),
        precision=lax.Precision.HIGHEST,
        preferred_element_type=jnp.float32,
    )
    weight_part = rep_reduce_scatter(weight_terms, jnp.float32)
    bias_part = jnp.sum(grad_block.astype(jnp.float32), axis=0)
    gathered = lax.all_gather(jnp.concatenate([weight_part, bias_part[None, :]], axis=0), "blk")
    totals = gathered[0]
    for block in range(1, blocks):
        totals = totals + gathered[block]
    returned = [jnp.zeros((half_rows, partition.shape[1]), jnp.float32) for _ in range(2)]
    for slot in range(pair_slots):
        partial = lax.dot_general(
            adjacency[slot],
            grad_block,
            (((0,), (0,)), ((), ())),
            preferred_element_type=jnp.float32,
        ).astype(jnp.bfloat16)
        for half in range(2):
            got = lax.ppermute(
                partial[half * half_rows:(half + 1) * half_rows],
                both_axes,
                source_pairs(blocks, replicas, slot, half, True),
            )
            returned[half] = returned[half] + got.astype(jnp.float32)
    partial_grad = jnp.concatenate(returned, axis=0)
    grad_hw = rep_reduce_scatter(partial_grad, jnp.bfloat16).astype(jnp.bfloat16)
    grad_feats = lax.dot_general(
        grad_hw, weight, (((1,), (1,)), ((), ())), preferred_element_type=jnp.float32
    ).astype(jnp.bfloat16)
    grad_weight = totals[:-1]
    grad_bias = totals[-1]
    return (out, grad_feats, grad_weight, grad_bias)


def solution(mesh):
    in_specs = (
        P(("blk", "rep"), None),
        P(),
        P(),
        P(("blk", "rep"), None),
        P("blk", "rep", None, None, None, None),
        P("blk", "rep", None, None),
        P("blk", "rep", None, None),
        P("blk", "rep", None),
    )
    out_specs = (P(("blk", "rep"), None), P(("blk", "rep"), None), P("rep", None), P())
    return jax.shard_map(body, mesh=mesh, in_specs=in_specs, out_specs=out_specs, check_vma=False)
```

```python
import jax
import jax.numpy as jnp
from jax import lax
from jax.sharding import PartitionSpec as P


def dense_adjacency(tile_vals, tile_row, tile_col, live, tiles_per_part):
    entries, tile_size, _ = tile_vals.shape
    cells = tiles_per_part * tiles_per_part
    cell_of_entry = tile_row * tiles_per_part + tile_col
    alive = jnp.arange(entries) < live
    select = (cell_of_entry[None, :] == jnp.arange(cells)[:, None]) & alive[None, :]
    placed = jnp.dot(
        select.astype(tile_vals.dtype),
        tile_vals.reshape(entries, tile_size * tile_size),
        preferred_element_type=jnp.float32,
    ).astype(tile_vals.dtype)
    placed = placed.reshape(tiles_per_part, tiles_per_part, tile_size, tile_size)
    side = tiles_per_part * tile_size
    return placed.transpose(0, 2, 1, 3).reshape(side, side)


def rep_reduce_scatter(x, wire_dtype):
    replicas = lax.axis_size("rep")
    rep_index = lax.axis_index("rep")
    bit_count = (replicas - 1).bit_length()
    rows = x.shape[0] // replicas
    current = x.reshape((2,) * bit_count + (rows,) + x.shape[1:])
    remaining = list(reversed(range(bit_count)))
    order = [0] + list(range(2, bit_count)) + [1] if bit_count > 2 else list(range(bit_count))
    for bit in order:
        axis = remaining.index(bit)
        mine = (rep_index >> bit) & 1
        keep = lax.dynamic_index_in_dim(current, mine, axis, keepdims=False)
        send = lax.dynamic_index_in_dim(current, 1 - mine, axis, keepdims=False)
        partner = [(i, i ^ (1 << bit)) for i in range(replicas)]
        got = lax.ppermute(send.astype(wire_dtype), "rep", partner)
        current = keep + got.astype(jnp.float32)
        remaining.remove(bit)
    return current


def rep_all_gather(x, order):
    replicas = lax.axis_size("rep")
    rep_index = lax.axis_index("rep")
    current = x
    held = []
    for bit in order:
        partner = [(i, i ^ (1 << bit)) for i in range(replicas)]
        got = lax.ppermute(current, "rep", partner)
        upper = ((rep_index >> bit) & 1) == 1
        low = jnp.where(upper, got, current)
        high = jnp.where(upper, current, got)
        held = sorted(held + [bit], reverse=True)
        current = jnp.stack([low, high], axis=held.index(bit))
    return current.reshape((-1,) + x.shape[1:])


def blk_all_reduce(x):
    blocks = lax.axis_size("blk")
    step = 1
    while step < blocks:
        x = x + lax.ppermute(x, "blk", [(i, i ^ step) for i in range(blocks)])
        step <<= 1
    return x


def source_pairs(blocks, replicas, slot, half, backward):
    pairs = []
    for b in range(blocks):
        for r in range(replicas):
            src_rep = r if half == 0 else replicas - 1 - r
            src = ((b - r - slot * replicas) % blocks) * replicas + src_rep
            dst = b * replicas + r
            pairs.append((dst, src) if backward else (src, dst))
    return pairs


def activation(pre_act, cotangent):
    logistic = jax.nn.sigmoid(pre_act)
    result = (pre_act * logistic).astype(jnp.bfloat16)
    grad_pre = (
        cotangent.astype(jnp.float32) * logistic * (1.0 + pre_act * (1.0 - logistic))
    ).astype(jnp.bfloat16)
    return (result, grad_pre)


def body(feats, weight, bias, grad_out, tile_values, tile_rows, tile_cols, tile_count):
    replicas = lax.axis_size("rep")
    blocks = lax.axis_size("blk")
    tile_size = tile_values.shape[-1]
    pair_slots = tile_values.shape[2]
    values_here = tile_values[0, 0]
    rows_here = tile_rows[0, 0]
    cols_here = tile_cols[0, 0]
    counts_here = tile_count[0, 0]
    partition = lax.all_gather(feats, "rep", axis=0, tiled=True)
    part_rows = partition.shape[0]
    half_rows = part_rows // 2
    tiles_per_part = part_rows // tile_size
    both_axes = ("blk", "rep")
    sources = []
    for slot in range(pair_slots):
        halves = [
            lax.ppermute(
                partition[half * half_rows:(half + 1) * half_rows],
                both_axes,
                source_pairs(blocks, replicas, slot, half, False),
            )
            for half in range(2)
        ]
        sources.append(jnp.concatenate(halves, axis=0))
    adjacency = [
        dense_adjacency(
            values_here[slot], rows_here[slot], cols_here[slot], counts_here[slot], tiles_per_part
        )
        for slot in range(pair_slots)
    ]
    aggregated_feats = jnp.zeros(partition.shape, jnp.float32)
    for slot in range(pair_slots):
        aggregated_feats = aggregated_feats + jnp.dot(
            adjacency[slot], sources[slot], preferred_element_type=jnp.float32
        )
    aggregate = jnp.dot(
        aggregated_feats,
        weight.astype(jnp.float32),
        precision=lax.Precision.HIGHEST,
        preferred_element_type=jnp.float32,
    )
    aggregate_rows = rep_reduce_scatter(aggregate, jnp.bfloat16)
    out, grad_rows = activation(aggregate_rows + bias, grad_out)
    grad_block = rep_all_gather(grad_rows, [1, 3, 2, 0])
    weight_terms = lax.dot_general(
        aggregated_feats,
        grad_block.astype(jnp.float32),
        (((0,), (0,)), ((), ())),
        precision=lax.Precision.HIGHEST,
        preferred_element_type=jnp.float32,
    )
    weight_part = rep_reduce_scatter(weight_terms, jnp.float32)
    bias_part = jnp.sum(grad_block.astype(jnp.float32), axis=0)
    totals = blk_all_reduce(jnp.concatenate([weight_part, bias_part[None, :]], axis=0))
    returned = [jnp.zeros((half_rows, partition.shape[1]), jnp.float32) for _ in range(2)]
    for slot in range(pair_slots):
        partial = lax.dot_general(
            adjacency[slot],
            grad_block,
            (((0,), (0,)), ((), ())),
            preferred_element_type=jnp.float32,
        ).astype(jnp.bfloat16)
        for half in range(2):
            got = lax.ppermute(
                partial[half * half_rows:(half + 1) * half_rows],
                both_axes,
                source_pairs(blocks, replicas, slot, half, True),
            )
            returned[half] = returned[half] + got.astype(jnp.float32)
    partial_grad = jnp.concatenate(returned, axis=0)
    grad_hw = rep_reduce_scatter(partial_grad, jnp.bfloat16).astype(jnp.bfloat16)
    grad_feats = lax.dot_general(
        grad_hw, weight, (((1,), (1,)), ((), ())), preferred_element_type=jnp.float32
    ).astype(jnp.bfloat16)
    grad_weight = totals[:-1]
    grad_bias = totals[-1]
    return (out, grad_feats, grad_weight, grad_bias)


def solution(mesh):
    in_specs = (
        P(("blk", "rep"), None),
        P(),
        P(),
        P(("blk", "rep"), None),
        P("blk", "rep", None, None, None, None),
        P("blk", "rep", None, None),
        P("blk", "rep", None, None),
        P("blk", "rep", None),
    )
    out_specs = (P(("blk", "rep"), None), P(("blk", "rep"), None), P("rep", None), P())
    return jax.shard_map(body, mesh=mesh, in_specs=in_specs, out_specs=out_specs, check_vma=False)
```

```python
import jax
import jax.numpy as jnp
from jax import lax
from jax.sharding import PartitionSpec as P


def dense_adjacency(tile_vals, tile_row, tile_col, live, tiles_per_part):
    entries, tile_size, _ = tile_vals.shape
    cells = tiles_per_part * tiles_per_part
    cell_of_entry = tile_row * tiles_per_part + tile_col
    alive = jnp.arange(entries) < live
    select = (cell_of_entry[None, :] == jnp.arange(cells)[:, None]) & alive[None, :]
    placed = jnp.dot(
        select.astype(tile_vals.dtype),
        tile_vals.reshape(entries, tile_size * tile_size),
        preferred_element_type=jnp.float32,
    ).astype(tile_vals.dtype)
    placed = placed.reshape(tiles_per_part, tiles_per_part, tile_size, tile_size)
    side = tiles_per_part * tile_size
    return placed.transpose(0, 2, 1, 3).reshape(side, side)


def rep_reduce_scatter(x, wire_dtype):
    replicas = lax.axis_size("rep")
    rep_index = lax.axis_index("rep")
    bit_count = (replicas - 1).bit_length()
    rows = x.shape[0] // replicas
    current = x.reshape((2,) * bit_count + (rows,) + x.shape[1:])
    remaining = list(reversed(range(bit_count)))
    order = [0] + list(range(2, bit_count)) + [1] if bit_count > 2 else list(range(bit_count))
    for bit in order:
        axis = remaining.index(bit)
        mine = (rep_index >> bit) & 1
        keep = lax.dynamic_index_in_dim(current, mine, axis, keepdims=False)
        send = lax.dynamic_index_in_dim(current, 1 - mine, axis, keepdims=False)
        partner = [(i, i ^ (1 << bit)) for i in range(replicas)]
        got = lax.ppermute(send.astype(wire_dtype), "rep", partner)
        current = keep + got.astype(jnp.float32)
        remaining.remove(bit)
    return current


def blk_all_reduce(x):
    blocks = lax.axis_size("blk")
    step = 1
    while step < blocks:
        x = x + lax.ppermute(x, "blk", [(i, i ^ step) for i in range(blocks)])
        step <<= 1
    return x


def source_pairs(blocks, replicas, slot, half, backward):
    pairs = []
    for b in range(blocks):
        for r in range(replicas):
            src_rep = r if half == 0 else replicas - 1 - r
            src = ((b - r - slot * replicas) % blocks) * replicas + src_rep
            dst = b * replicas + r
            pairs.append((dst, src) if backward else (src, dst))
    return pairs


def activation(pre_act, cotangent):
    logistic = jax.nn.sigmoid(pre_act)
    result = (pre_act * logistic).astype(jnp.bfloat16)
    grad_pre = (
        cotangent.astype(jnp.float32) * logistic * (1.0 + pre_act * (1.0 - logistic))
    ).astype(jnp.bfloat16)
    return (result, grad_pre)


def body(feats, weight, bias, grad_out, tile_values, tile_rows, tile_cols, tile_count):
    replicas = lax.axis_size("rep")
    blocks = lax.axis_size("blk")
    tile_size = tile_values.shape[-1]
    pair_slots = tile_values.shape[2]
    values_here = tile_values[0, 0]
    rows_here = tile_rows[0, 0]
    cols_here = tile_cols[0, 0]
    counts_here = tile_count[0, 0]
    partition = lax.all_gather(feats, "rep", axis=0, tiled=True)
    part_rows = partition.shape[0]
    half_rows = part_rows // 2
    tiles_per_part = part_rows // tile_size
    both_axes = ("blk", "rep")
    sources = []
    for slot in range(pair_slots):
        halves = [
            lax.ppermute(
                partition[half * half_rows:(half + 1) * half_rows],
                both_axes,
                source_pairs(blocks, replicas, slot, half, False),
            )
            for half in range(2)
        ]
        sources.append(jnp.concatenate(halves, axis=0))
    adjacency = [
        dense_adjacency(
            values_here[slot], rows_here[slot], cols_here[slot], counts_here[slot], tiles_per_part
        )
        for slot in range(pair_slots)
    ]
    aggregated_feats = jnp.zeros(partition.shape, jnp.float32)
    for slot in range(pair_slots):
        aggregated_feats = aggregated_feats + jnp.dot(
            adjacency[slot], sources[slot], preferred_element_type=jnp.float32
        )
    feats_high = aggregated_feats.astype(jnp.bfloat16)
    feats_low = (aggregated_feats - feats_high.astype(jnp.float32)).astype(jnp.bfloat16)
    aggregate = jnp.dot(feats_high, weight, preferred_element_type=jnp.float32) + jnp.dot(
        feats_low, weight, preferred_element_type=jnp.float32
    )
    aggregate_rows = rep_reduce_scatter(aggregate, jnp.bfloat16)
    out, grad_rows = activation(aggregate_rows + bias, grad_out)
    grad_block = lax.all_gather(grad_rows, "rep", axis=0, tiled=True)
    weight_terms = sum(
        lax.dot_general(
            part, grad_block, (((0,), (0,)), ((), ())), preferred_element_type=jnp.float32
        )
        for part in (feats_high, feats_low)
    )
    weight_part = rep_reduce_scatter(weight_terms, jnp.float32)
    bias_part = jnp.sum(grad_block.astype(jnp.float32), axis=0)
    totals = blk_all_reduce(jnp.concatenate([weight_part, bias_part[None, :]], axis=0))
    returned = [jnp.zeros((half_rows, partition.shape[1]), jnp.float32) for _ in range(2)]
    for slot in range(pair_slots):
        partial = lax.dot_general(
            adjacency[slot],
            grad_block,
            (((0,), (0,)), ((), ())),
            preferred_element_type=jnp.float32,
        ).astype(jnp.bfloat16)
        for half in range(2):
            got = lax.ppermute(
                partial[half * half_rows:(half + 1) * half_rows],
                both_axes,
                source_pairs(blocks, replicas, slot, half, True),
            )
            returned[half] = returned[half] + got.astype(jnp.float32)
    partial_grad = jnp.concatenate(returned, axis=0)
    grad_hw = rep_reduce_scatter(partial_grad, jnp.bfloat16).astype(jnp.bfloat16)
    grad_feats = lax.dot_general(
        grad_hw, weight, (((1,), (1,)), ((), ())), preferred_element_type=jnp.float32
    ).astype(jnp.bfloat16)
    grad_weight = totals[:-1]
    grad_bias = totals[-1]
    return (out, grad_feats, grad_weight, grad_bias)


def solution(mesh):
    in_specs = (
        P(("blk", "rep"), None),
        P(),
        P(),
        P(("blk", "rep"), None),
        P("blk", "rep", None, None, None, None),
        P("blk", "rep", None, None),
        P("blk", "rep", None, None),
        P("blk", "rep", None),
    )
    out_specs = (P(("blk", "rep"), None), P(("blk", "rep"), None), P("rep", None), P())
    return jax.shard_map(body, mesh=mesh, in_specs=in_specs, out_specs=out_specs, check_vma=False)
```
